256 devices in a mesh: seq: 32 (over y, z_hi, core), head: 8 (over z_lo, x).
Axes of the slice: x: 4, y: 4, z: 8 (z_hi: 4, z_lo: 2; z = z_hi * 2 + z_lo), core: 2. Of those that a mesh axis runs over, the one named last changes fastest.
Arguments:
- xin: bfloat16 [16384, 8192], P('seq', 'head'), may hold values from -6 to 6
- gate_z: bfloat16 [16384, 8192], P('seq', 'head'), may hold values from -6 to 6
- b_proj: bfloat16 [16384, 8, 256], P('seq', 'head'), may hold values from -0.375 to 0.375
- c_proj: bfloat16 [16384, 8, 256], P('seq', 'head'), may hold values from -0.375 to 0.375
- log_retain: float32 [16384, 128], P('seq', 'head'), may hold values from -2 to 0, as said below
- skip_d: float32 [128], P('head'), may hold values from 0.5 to 2
- norm_gain: float32 [8192], P('head'), may hold values from 0.5 to 1.5
- w_out: bfloat16 [8192, 4096], P('head', 'seq'), may hold values from -0.0625 to 0.0625
- residual: bfloat16 [16384, 4096], P(('seq', 'head')), may hold values from -24 to 24
- refusal: float32 [4096], replicated, may hold values from -6 to 6
- stream_gain: float32 [4096], replicated, may hold values from 0.5 to 1.5
- w_in: bfloat16 [4096, 8192], P('seq', 'head'), may hold values from -0.09375 to 0.09375
Outputs:
- stream: bfloat16 [16384, 4096], P(('seq', 'head'))
- next_x: bfloat16 [16384, 8192], P('seq', 'head')
The draws below stay inside these ranges and needn't reach their ends.
Inputs may be any that keep to these rules, and one draw needn't show every extreme that they name: `log_retain`: every entry is negative.
All inputs are finite; a program needn't handle non-finite values.
Results may differ from the reference program's by a relative error of at most 0.02.
Values may be sent and summed in bfloat16 or wider, within the bound.
No kernel may reach another device: no remote copies, remote signals or barrier semaphores. Data moves between devices by JAX's collectives and lax.ppermute only.
A program may use at most 192 MiB of HBM per device.

```python
import jax
import jax.numpy as jnp
from jax import lax

D = 4096
HEADS = 128
HEAD_DIM = 64
STATE = 256
GROUPS = 8
SPAN = 256
TOK_DEV = 512
INNER = 8192
PROMPT_TOKENS = 16384
N_HEAD = 8


def draw_log_retain(key, part):
    random_key_sequence = jax.random.split(key, 7)
    fast_heads = jax.random.uniform(random_key_sequence[0], (HEADS,)) < 0.5
    fast_rate = jnp.exp(jax.random.uniform(random_key_sequence[1], (HEADS,), minval=jnp.log(0.03), maxval=jnp.log(0.1)))
    slow_rate = jax.random.uniform(random_key_sequence[2], (HEADS,), minval=0.2, maxval=0.6) / PROMPT_TOKENS
    head_decay_rate = jnp.where(fast_heads, fast_rate, slow_rate)
    token_multiplier = jnp.exp(jax.random.uniform(random_key_sequence[3], (PROMPT_TOKENS, HEADS), minval=jnp.log(0.5), maxval=jnp.log(2.0)))
    partition_factor = jnp.exp(jax.random.uniform(random_key_sequence[4], (PROMPT_TOKENS // TOK_DEV, 1, HEADS), minval=jnp.log(0.5), maxval=jnp.log(2.0)))
    partition_factor = jnp.broadcast_to(partition_factor, (PROMPT_TOKENS // TOK_DEV, TOK_DEV, HEADS)).reshape(PROMPT_TOKENS, HEADS)
    spike_selections = jax.random.randint(random_key_sequence[5], (2,), 0, PROMPT_TOKENS)
    token_positions = jnp.arange(PROMPT_TOKENS, dtype=jnp.int32)
    spike_count = jnp.sum((token_positions[:, None] == spike_selections[None, :]).astype(jnp.float32), axis=1)
    spike_loss = jax.random.uniform(random_key_sequence[6], (PROMPT_TOKENS, 1), minval=0.22, maxval=0.69)
    return -(head_decay_rate[None, :] * token_multiplier * partition_factor) - spike_count[:, None] * spike_loss


def direction_draw(key):
    return jnp.clip(jax.random.normal(jax.random.fold_in(key, 11), (D,), jnp.float32), -6.0, 6.0)


def draw_refusal(key, part):
    return direction_draw(key)


def draw_residual(key, part):
    direction = direction_draw(key)
    weight_along = 0.8 * jax.random.normal(jax.random.fold_in(key, 12), (PROMPT_TOKENS, 1), jnp.float32)
    base_values = jax.random.normal(jax.random.fold_in(key, 13), (PROMPT_TOKENS, D), jnp.float32)
    return jnp.clip(base_values + weight_along * direction[None, :], -24.0, 24.0).astype(jnp.bfloat16)


def level_of(rng, shape, shards, least, high):
    loudness, own = 1.0, jax.random.fold_in(rng, 6)
    for axis_at, shards_of in shards:
        heights = jnp.exp(jax.random.uniform(jax.random.fold_in(own, axis_at), (shards_of,), jnp.float32, least / len(shards), high / len(shards)))
        loudness = loudness * jnp.repeat(heights, shape[axis_at] // shards_of).reshape([-1 if axis == axis_at else 1 for axis in range(len(shape))])
    return loudness


def gaussian(own_key, shape, scale, reach, shards=(), kind=jnp.bfloat16):
    drawn = scale * jax.random.normal(own_key, shape, jnp.float32)
    if shards:
        drawn = drawn * level_of(own_key, shape, shards, -0.22, 0.18)
    return jnp.clip(drawn, -reach, reach).astype(kind)


def setup_inputs(seed: int = 0) -> dict:
    keys = jax.random.split(jax.random.key(seed), 13)
    xin = gaussian(keys[0], (PROMPT_TOKENS, INNER), 1.0, 6.0, ((0, 32), (1, 8)))
    gate_z = gaussian(keys[1], (PROMPT_TOKENS, INNER), 1.0, 6.0, ((0, 32), (1, 8)))
    b_proj = gaussian(keys[2], (PROMPT_TOKENS, GROUPS, STATE), (STATE ** -0.5), 0.375, ((0, 32), (1, 8)))
    c_proj = gaussian(keys[3], (PROMPT_TOKENS, GROUPS, STATE), (STATE ** -0.5), 0.375, ((0, 32), (1, 8)))
    log_retain = draw_log_retain(jax.random.fold_in(keys[12], 71), 0)
    skip_d = jnp.clip(0.5 + 1.5 * jax.random.uniform(keys[5], (HEADS,), jnp.float32) ** level_of(keys[5], (HEADS,), ((0, 8),), -0.2, 0.2), 0.5, 2.0)
    norm_gain = jnp.clip(1.0 + 0.1 * jax.random.normal(keys[6], (INNER,), jnp.float32), 0.5, 1.5)
    w_out = gaussian(keys[7], (INNER, D), INNER ** -0.5, 0.0625, ((0, 8), (1, 32)))
    residual = draw_residual(jax.random.fold_in(keys[12], 71), 0)
    refusal = draw_refusal(jax.random.fold_in(keys[12], 71), 0)
    stream_gain = jnp.clip(1.0 + 0.1 * jax.random.normal(keys[10], (D,), jnp.float32), 0.5, 1.5)
    w_in = gaussian(keys[11], (D, INNER), D ** -0.5, 0.09375, ((0, 32), (1, 8)))
    return {"xin": xin, "gate_z": gate_z, "b_proj": b_proj, "c_proj": c_proj, "log_retain": log_retain, "skip_d": skip_d, "norm_gain": norm_gain, "w_out": w_out, "residual": residual, "refusal": refusal, "stream_gain": stream_gain, "w_in": w_in}


def span_step(carry_state, inputs, skip_d, norm_gain):
    x_block, z_block, b_block, c_block, retain_block = inputs
    per_group = HEADS // GROUPS
    cum = jnp.cumsum(retain_block, axis=0)
    cum_heads = jnp.transpose(cum, (1, 0))
    scores = jnp.einsum('lgn,sgn->gls', c_block.astype(jnp.float32), b_block.astype(jnp.float32))
    scores = jnp.repeat(scores, per_group, axis=0)
    later_pos = lax.broadcasted_iota(jnp.int32, (SPAN, SPAN), 0)
    earlier_pos = lax.broadcasted_iota(jnp.int32, (SPAN, SPAN), 1)
    causal = later_pos >= earlier_pos
    gap = cum_heads[:, :, None] - cum_heads[:, None, :]
    mixing = (jnp.where(causal, jnp.exp(jnp.where(causal, gap, 0.0)), 0.0) * scores).astype(jnp.bfloat16)
    x_float = x_block.astype(jnp.float32)
    intra = jnp.einsum('hls,shp->lhp', mixing.astype(jnp.float32), x_float)
    b_heads = jnp.repeat(b_block, per_group, axis=1)
    c_heads = jnp.repeat(c_block, per_group, axis=1).astype(jnp.float32)
    carried = jnp.einsum('lhn,hnp->lhp', c_heads, carry_state, precision=lax.Precision.HIGHEST)
    carried = carried * jnp.exp(cum)[:, :, None]
    tail_decay = jnp.exp(cum_heads[:, -1:] - cum_heads)
    weighted_b = (b_heads.astype(jnp.float32) * jnp.transpose(tail_decay, (1, 0))[:, :, None]).astype(jnp.bfloat16)
    block_state = jnp.einsum('lhn,lhp->hnp', weighted_b.astype(jnp.float32), x_float)
    new_state = jnp.exp(cum_heads[:, -1])[:, None, None] * carry_state + block_state
    mixed = intra + carried + skip_d[None, :, None] * x_float
    gated = mixed * jax.nn.silu(z_block.astype(jnp.float32))
    grouped = gated.reshape(SPAN, GROUPS, per_group * HEAD_DIM)
    grouped = grouped * lax.rsqrt(lax.optimization_barrier(jnp.mean(grouped * grouped, axis=-1, keepdims=True)) + 1e-05)
    ssd_out = (grouped.reshape(SPAN, INNER) * norm_gain[None, :]).astype(jnp.bfloat16)
    return (new_state, ssd_out)

def reference(xin, gate_z, b_proj, c_proj, log_retain, skip_d, norm_gain, w_out, residual, refusal, stream_gain, w_in):
    block_total = PROMPT_TOKENS // SPAN
    x_blocks = xin.reshape(block_total, SPAN, HEADS, HEAD_DIM)
    z_blocks = gate_z.reshape(block_total, SPAN, HEADS, HEAD_DIM)
    b_blocks = b_proj.reshape(block_total, SPAN, GROUPS, STATE)
    c_blocks = c_proj.reshape(block_total, SPAN, GROUPS, STATE)
    retain_blocks = log_retain.reshape(block_total, SPAN, HEADS)
    start_state = jnp.zeros((HEADS, STATE, HEAD_DIM), jnp.float32)

    def scan_step(carry_state, inputs):
        return span_step(carry_state, inputs, skip_d, norm_gain)
    unused_state, ssd_blocks = lax.scan(scan_step, start_state, (x_blocks, z_blocks, b_blocks, c_blocks, retain_blocks))
    ssd_out = ssd_blocks.reshape(PROMPT_TOKENS, INNER)
    block_width = INNER // N_HEAD
    mixer_out = jnp.zeros((PROMPT_TOKENS, D), jnp.float32)
    for block_index in range(N_HEAD):
        lower = block_index * block_width
        partial_value = jnp.dot(ssd_out[:, lower:lower + block_width], w_out[lower:lower + block_width, :], preferred_element_type=jnp.float32).astype(jnp.bfloat16)
        mixer_out = mixer_out + partial_value.astype(jnp.float32)
    unit = refusal / jnp.sqrt(jnp.sum(refusal * refusal) + 1e-06)
    hidden = residual.astype(jnp.float32) + mixer_out
    coef = jnp.dot(hidden, unit, precision=lax.Precision.HIGHEST)
    stream = (hidden - coef[:, None] * unit[None, :]).astype(jnp.bfloat16)
    stream_float = stream.astype(jnp.float32)
    normed = (stream_float * lax.rsqrt(lax.optimization_barrier(jnp.mean(stream_float * stream_float, axis=-1, keepdims=True)) + 1e-05) * stream_gain[None, :]).astype(jnp.bfloat16)
    next_x = jnp.dot(normed, w_in, preferred_element_type=jnp.float32).astype(jnp.bfloat16)
    return (stream, next_x)
```

```python
import jax
import jax.numpy as jnp
from jax import lax
from jax.sharding import PartitionSpec as P

SPAN = 256


def shift_scan(decay, state, axis):
    devices = lax.axis_size(axis)

    def shifted(parts, distance):
        pairs = [(i, i + distance) for i in range(devices - distance)]
        a, s = parts
        return (
            lax.ppermute(a, axis, pairs),
            lax.ppermute(s.astype(jnp.bfloat16), axis, pairs).astype(jnp.float32),
        )

    acc = shifted((decay, state), 1)
    distance = 1
    while distance < devices:
        acc = carry_combine(shifted(acc, distance), acc)
        distance *= 2
    return acc


def carry_combine(earlier, later):
    decay_early, state_early = earlier
    decay_later, state_later = later
    return (
        decay_early + decay_later,
        jnp.exp(decay_later)[:, None, None] * state_early + state_later,
    )


def body(
    xin,
    gate_z,
    b_proj,
    c_proj,
    log_retain,
    skip_d,
    norm_gain,
    w_out,
    residual,
    refusal,
    stream_gain,
    w_in,
):
    seq_rows, channels = xin.shape
    head_count = log_retain.shape[1]
    head_width = channels // head_count
    group_count = b_proj.shape[1]
    state_width = b_proj.shape[2]
    per_group = head_count // group_count
    block_count = seq_rows // SPAN
    inputs = xin.reshape(block_count, SPAN, head_count, head_width)
    b_grouped = b_proj.reshape(block_count, SPAN, group_count, state_width)
    c_grouped = c_proj.reshape(block_count, SPAN, group_count, state_width)
    scores = jnp.einsum("klgn,ksgn->kgls", c_grouped, b_grouped, preferred_element_type=jnp.float32)
    scores = jnp.repeat(scores, per_group, axis=1)
    cum = jnp.cumsum(log_retain.reshape(block_count, SPAN, head_count), axis=1)
    cum_heads = jnp.transpose(cum, (0, 2, 1))
    later_pos = lax.broadcasted_iota(jnp.int32, (SPAN, SPAN), 0)
    earlier_pos = lax.broadcasted_iota(jnp.int32, (SPAN, SPAN), 1)
    causal = later_pos >= earlier_pos
    gap = cum_heads[:, :, :, None] - cum_heads[:, :, None, :]
    mixing = (jnp.where(causal, jnp.exp(jnp.where(causal, gap, 0.0)), 0.0) * scores).astype(
        jnp.bfloat16
    )
    intra = jnp.einsum("khls,kshp->klhp", mixing, inputs, preferred_element_type=jnp.float32)
    tail_decay = jnp.exp(cum_heads[:, :, -1:] - cum_heads)
    b_heads = jnp.repeat(b_grouped, per_group, axis=2)
    weighted_b = (
        b_heads.astype(jnp.float32) * jnp.transpose(tail_decay, (0, 2, 1))[..., None]
    ).astype(jnp.bfloat16)
    block_state = jnp.einsum(
        "klhn,klhp->khnp", weighted_b, inputs, preferred_element_type=jnp.float32
    )
    block_decay = cum_heads[:, :, -1]

    def advance(carried_state, pair):
        decay_here, state_here = pair
        return (jnp.exp(decay_here)[:, None, None] * carried_state + state_here, carried_state)

    zero_state = jnp.zeros((head_count, state_width, head_width), jnp.float32)
    device_state, local_starts = lax.scan(advance, zero_state, (block_decay, block_state))
    device_decay = jnp.sum(block_decay, axis=0)
    total_decay, incoming = shift_scan(device_decay, device_state, "seq")
    before_block = jnp.cumsum(block_decay, axis=0) - block_decay
    starts = local_starts + jnp.exp(before_block)[:, :, None, None] * incoming[None]
    c_heads = jnp.repeat(c_grouped, per_group, axis=2).astype(jnp.float32)
    carried = jnp.einsum("klhn,khnp->klhp", c_heads, starts, precision=lax.Precision.HIGHEST)
    carried = carried * jnp.exp(cum)[..., None]
    mixed = intra + carried + skip_d[None, None, :, None] * inputs.astype(jnp.float32)
    gated = mixed * jax.nn.silu(
        gate_z.reshape(block_count, SPAN, head_count, head_width).astype(jnp.float32)
    )
    grouped = gated.reshape(seq_rows, group_count, per_group * head_width)
    grouped = grouped * lax.rsqrt(jnp.mean(grouped * grouped, axis=-1, keepdims=True) + 1e-05)
    ssd_out = (grouped.reshape(seq_rows, channels) * norm_gain[None, :]).astype(jnp.bfloat16)
    w_in_all = lax.all_gather(w_in, "seq", axis=0, tiled=True)
    ssd_out, w_in_all = lax.optimization_barrier((ssd_out, w_in_all))
    partial_sum = jnp.dot(
        ssd_out,
        lax.all_gather(w_out, "seq", axis=1, tiled=True),
        preferred_element_type=jnp.float32,
    )
    mixer_out = lax.psum_scatter(
        partial_sum.astype(jnp.bfloat16), "head", scatter_dimension=0, tiled=True
    ).astype(jnp.float32)
    unit = refusal / jnp.sqrt(jnp.sum(refusal * refusal) + 1e-06)
    hidden = residual.astype(jnp.float32) + mixer_out
    coef = jnp.dot(hidden, unit, precision=lax.Precision.HIGHEST)
    stream = (hidden - coef[:, None] * unit[None, :]).astype(jnp.bfloat16)
    stream_float = stream.astype(jnp.float32)
    normed = (
        stream_float
        * lax.rsqrt(jnp.mean(stream_float * stream_float, axis=-1, keepdims=True) + 1e-05)
        * stream_gain[None, :]
    ).astype(jnp.bfloat16)
    all_rows = lax.all_gather(normed, "head", axis=0, tiled=True)
    next_float = jnp.dot(
        all_rows,
        w_in_all,
        preferred_element_type=jnp.float32,
    )
    return (stream, next_float.astype(jnp.bfloat16))


def solution(mesh):
    in_specs = (
        P("seq", "head"),
        P("seq", "head"),
        P("seq", "head", None),
        P("seq", "head", None),
        P("seq", "head"),
        P("head"),
        P("head"),
        P("head", "seq"),
        P(("seq", "head"), None),
        P(),
        P(),
        P("seq", "head"),
    )
    out_specs = (P(("seq", "head"), None), P("seq", "head"))
    return jax.shard_map(body, mesh=mesh, in_specs=in_specs, out_specs=out_specs, check_vma=False)
```

```python
import jax
import jax.numpy as jnp
from jax import lax
from jax.sharding import Mesh, PartitionSpec as P

SPAN = 256


def shift_scan(decay, state, axis):
    devices = lax.axis_size(axis)

    def shifted(parts, distance):
        pairs = [(i, i + distance) for i in range(devices - distance)]
        a, s = parts
        return (
            lax.ppermute(a, axis, pairs),
            lax.ppermute(s.astype(jnp.bfloat16), axis, pairs).astype(jnp.float32),
        )

    acc = shifted((decay, state), 1)
    distance = 1
    while distance < devices:
        acc = carry_combine(shifted(acc, distance), acc)
        distance *= 2
    return acc


def gather_pairs(part, axis):
    across = lax.all_gather(part, "chip", axis=0)
    both = lax.all_gather(across, "core", axis=1)
    both = jnp.moveaxis(both, (0, 1), (axis, axis + 1))
    shape = list(part.shape)
    shape[axis] = -1
    return both.reshape(shape)


def carry_combine(earlier, later):
    decay_early, state_early = earlier
    decay_later, state_later = later
    return (
        decay_early + decay_later,
        jnp.exp(decay_later)[:, None, None] * state_early + state_later,
    )


def body(
    xin,
    gate_z,
    b_proj,
    c_proj,
    log_retain,
    skip_d,
    norm_gain,
    w_out,
    residual,
    refusal,
    stream_gain,
    w_in,
):
    seq_rows, channels = xin.shape
    head_count = log_retain.shape[1]
    head_width = channels // head_count
    group_count = b_proj.shape[1]
    state_width = b_proj.shape[2]
    per_group = head_count // group_count
    block_count = seq_rows // SPAN
    inputs = xin.reshape(block_count, SPAN, head_count, head_width)
    b_grouped = b_proj.reshape(block_count, SPAN, group_count, state_width)
    c_grouped = c_proj.reshape(block_count, SPAN, group_count, state_width)
    scores = jnp.einsum("klgn,ksgn->kgls", c_grouped, b_grouped, preferred_element_type=jnp.float32)
    scores = jnp.repeat(scores, per_group, axis=1)
    cum = jnp.cumsum(log_retain.reshape(block_count, SPAN, head_count), axis=1)
    cum_heads = jnp.transpose(cum, (0, 2, 1))
    later_pos = lax.broadcasted_iota(jnp.int32, (SPAN, SPAN), 0)
    earlier_pos = lax.broadcasted_iota(jnp.int32, (SPAN, SPAN), 1)
    causal = later_pos >= earlier_pos
    gap = cum_heads[:, :, :, None] - cum_heads[:, :, None, :]
    mixing = (jnp.where(causal, jnp.exp(jnp.where(causal, gap, 0.0)), 0.0) * scores).astype(
        jnp.bfloat16
    )
    intra = jnp.einsum("khls,kshp->klhp", mixing, inputs, preferred_element_type=jnp.float32)
    tail_decay = jnp.exp(cum_heads[:, :, -1:] - cum_heads)
    b_heads = jnp.repeat(b_grouped, per_group, axis=2)
    weighted_b = (
        b_heads.astype(jnp.float32) * jnp.transpose(tail_decay, (0, 2, 1))[..., None]
    ).astype(jnp.bfloat16)
    block_state = jnp.einsum(
        "klhn,klhp->khnp", weighted_b, inputs, preferred_element_type=jnp.float32
    )
    block_decay = cum_heads[:, :, -1]

    def advance(carried_state, pair):
        decay_here, state_here = pair
        return (jnp.exp(decay_here)[:, None, None] * carried_state + state_here, carried_state)

    zero_state = jnp.zeros((head_count, state_width, head_width), jnp.float32)
    device_state, local_starts = lax.scan(advance, zero_state, (block_decay, block_state))
    device_decay = jnp.sum(block_decay, axis=0)
    total_decay, incoming = shift_scan(device_decay, device_state, ("chip", "core"))
    before_block = jnp.cumsum(block_decay, axis=0) - block_decay
    starts = local_starts + jnp.exp(before_block)[:, :, None, None] * incoming[None]
    c_heads = jnp.repeat(c_grouped, per_group, axis=2).astype(jnp.float32)
    carried = jnp.einsum("klhn,khnp->klhp", c_heads, starts, precision=lax.Precision.HIGHEST)
    carried = carried * jnp.exp(cum)[..., None]
    mixed = intra + carried + skip_d[None, None, :, None] * inputs.astype(jnp.float32)
    gated = mixed * jax.nn.silu(
        gate_z.reshape(block_count, SPAN, head_count, head_width).astype(jnp.float32)
    )
    grouped = gated.reshape(seq_rows, group_count, per_group * head_width)
    grouped = grouped * lax.rsqrt(jnp.mean(grouped * grouped, axis=-1, keepdims=True) + 1e-05)
    ssd_out = (grouped.reshape(seq_rows, channels) * norm_gain[None, :]).astype(jnp.bfloat16)
    w_in_all = gather_pairs(w_in, 0)
    ssd_out, w_in_all = lax.optimization_barrier((ssd_out, w_in_all))
    partial_sum = jnp.dot(
        ssd_out,
        gather_pairs(w_out, 1),
        preferred_element_type=jnp.float32,
    )
    mixer_out = lax.psum_scatter(
        partial_sum.astype(jnp.bfloat16), ("zlo", "x"), scatter_dimension=0, tiled=True
    ).astype(jnp.float32)
    unit = refusal / jnp.sqrt(jnp.sum(refusal * refusal) + 1e-06)
    hidden = residual.astype(jnp.float32) + mixer_out
    coef = jnp.dot(hidden, unit, precision=lax.Precision.HIGHEST)
    stream = (hidden - coef[:, None] * unit[None, :]).astype(jnp.bfloat16)
    stream_float = stream.astype(jnp.float32)
    normed = (
        stream_float
        * lax.rsqrt(jnp.mean(stream_float * stream_float, axis=-1, keepdims=True) + 1e-05)
        * stream_gain[None, :]
    ).astype(jnp.bfloat16)
    all_rows = lax.all_gather(normed, ("zlo", "x"), axis=0, tiled=True)
    next_float = jnp.dot(
        all_rows,
        w_in_all,
        preferred_element_type=jnp.float32,
    )
    return (stream, next_float.astype(jnp.bfloat16))


def solution(mesh):
    in_specs = (
        P(("chip", "core"), ("zlo", "x")),
        P(("chip", "core"), ("zlo", "x")),
        P(("chip", "core"), ("zlo", "x"), None),
        P(("chip", "core"), ("zlo", "x"), None),
        P(("chip", "core"), ("zlo", "x")),
        P(("zlo", "x")),
        P(("zlo", "x")),
        P(("zlo", "x"), ("chip", "core")),
        P(("chip", "core", "zlo", "x"), None),
        P(),
        P(),
        P(("chip", "core"), ("zlo", "x")),
    )
    out_specs = (P(("chip", "core", "zlo", "x"), None), P(("chip", "core"), ("zlo", "x")))
    seq_size, head_size = mesh.devices.shape
    split = Mesh(
        mesh.devices.reshape(seq_size // 2, 2, 2, head_size // 2), ("chip", "core", "zlo", "x")
    )
    return jax.shard_map(body, mesh=split, in_specs=in_specs, out_specs=out_specs, check_vma=False)
```

```python
import jax
import jax.numpy as jnp
from jax import lax
from jax.sharding import PartitionSpec as P

SPAN = 256


def shift_scan(decay, state, axis):
    devices = lax.axis_size(axis)

    def shifted(parts, distance):
        pairs = [(i, i + distance) for i in range(devices - distance)]
        a, s = parts
        return (
            lax.ppermute(a, axis, pairs),
            lax.ppermute(s.astype(jnp.bfloat16), axis, pairs).astype(jnp.float32),
        )

    acc = shifted((decay, state), 1)
    distance = 1
    while distance < devices:
        acc = carry_combine(shifted(acc, distance), acc)
        distance *= 2
    return acc


def carry_combine(earlier, later):
    decay_early, state_early = earlier
    decay_later, state_later = later
    return (
        decay_early + decay_later,
        jnp.exp(decay_later).reshape((-1,) + (1,) * (state_later.ndim - 1)) * state_early
        + state_later,
    )


def body(
    xin,
    gate_z,
    b_proj,
    c_proj,
    log_retain,
    skip_d,
    norm_gain,
    w_out,
    residual,
    refusal,
    stream_gain,
    w_in,
):
    seq_rows, channels = xin.shape
    head_count = log_retain.shape[1]
    head_width = channels // head_count
    group_count = b_proj.shape[1]
    state_width = b_proj.shape[2]
    per_group = head_count // group_count
    block_count = seq_rows // SPAN
    inputs = xin.reshape(block_count, SPAN, head_count, head_width)
    b_grouped = b_proj.reshape(block_count, SPAN, group_count, state_width)
    c_grouped = c_proj.reshape(block_count, SPAN, group_count, state_width)
    scores = jnp.einsum("klgn,ksgn->kgls", c_grouped, b_grouped, preferred_element_type=jnp.float32)
    scores = jnp.repeat(scores, per_group, axis=1)
    cum = jnp.cumsum(log_retain.reshape(block_count, SPAN, head_count), axis=1)
    cum_heads = jnp.transpose(cum, (0, 2, 1))
    later_pos = lax.broadcasted_iota(jnp.int32, (SPAN, SPAN), 0)
    earlier_pos = lax.broadcasted_iota(jnp.int32, (SPAN, SPAN), 1)
    causal = later_pos >= earlier_pos
    gap = cum_heads[:, :, :, None] - cum_heads[:, :, None, :]
    mixing = (jnp.where(causal, jnp.exp(jnp.where(causal, gap, 0.0)), 0.0) * scores).astype(
        jnp.bfloat16
    )
    intra = jnp.einsum("khls,kshp->klhp", mixing, inputs, preferred_element_type=jnp.float32)
    tail_decay = jnp.exp(cum_heads[:, :, -1:] - cum_heads)
    b_heads = jnp.repeat(b_grouped, per_group, axis=2)
    weighted_b = (
        b_heads.astype(jnp.float32) * jnp.transpose(tail_decay, (0, 2, 1))[..., None]
    ).astype(jnp.bfloat16)
    block_state = jnp.einsum(
        "klhn,klhp->khnp", weighted_b, inputs, preferred_element_type=jnp.float32
    )
    block_decay = cum_heads[:, :, -1]

    def advance(carried_state, pair):
        decay_here, state_here = pair
        return (jnp.exp(decay_here)[:, None, None] * carried_state + state_here, carried_state)

    zero_state = jnp.zeros((head_count, state_width, head_width), jnp.float32)
    device_state, local_starts = lax.scan(advance, zero_state, (block_decay, block_state))
    device_decay = jnp.sum(block_decay, axis=0)
    total_decay, incoming = shift_scan(
        device_decay, device_state.reshape(head_count, state_width * head_width), "seq"
    )
    incoming = incoming.reshape(head_count, state_width, head_width)
    before_block = jnp.cumsum(block_decay, axis=0) - block_decay
    starts = local_starts + jnp.exp(before_block)[:, :, None, None] * incoming[None]
    c_heads = jnp.repeat(c_grouped, per_group, axis=2).astype(jnp.float32)
    carried = jnp.einsum("klhn,khnp->klhp", c_heads, starts, precision=lax.Precision.HIGHEST)
    carried = carried * jnp.exp(cum)[..., None]
    mixed = intra + carried + skip_d[None, None, :, None] * inputs.astype(jnp.float32)
    gated = mixed * jax.nn.silu(
        gate_z.reshape(block_count, SPAN, head_count, head_width).astype(jnp.float32)
    )
    grouped = gated.reshape(seq_rows, group_count, per_group * head_width)
    grouped = grouped * lax.rsqrt(jnp.mean(grouped * grouped, axis=-1, keepdims=True) + 1e-05)
    ssd_out = (grouped.reshape(seq_rows, channels) * norm_gain[None, :]).astype(jnp.bfloat16)
    w_in_all = lax.all_gather(w_in, "seq", axis=0, tiled=True)
    ssd_out, w_in_all = lax.optimization_barrier((ssd_out, w_in_all))
    partial_sum = jnp.dot(
        ssd_out,
        lax.all_gather(w_out, "seq", axis=1, tiled=True),
        preferred_element_type=jnp.float32,
    )
    mixer_out = lax.psum_scatter(
        partial_sum.astype(jnp.bfloat16), "head", scatter_dimension=0, tiled=True
    ).astype(jnp.float32)
    unit = refusal / jnp.sqrt(jnp.sum(refusal * refusal) + 1e-06)
    hidden = residual.astype(jnp.float32) + mixer_out
    coef = jnp.dot(hidden, unit, precision=lax.Precision.HIGHEST)
    stream = (hidden - coef[:, None] * unit[None, :]).astype(jnp.bfloat16)
    stream_float = stream.astype(jnp.float32)
    normed = (
        stream_float
        * lax.rsqrt(jnp.mean(stream_float * stream_float, axis=-1, keepdims=True) + 1e-05)
        * stream_gain[None, :]
    ).astype(jnp.bfloat16)
    all_rows = lax.all_gather(normed, "head", axis=0, tiled=True)
    next_float = jnp.dot(
        all_rows,
        w_in_all,
        preferred_element_type=jnp.float32,
    )
    return (stream, next_float.astype(jnp.bfloat16))


def solution(mesh):
    in_specs = (
        P("seq", "head"),
        P("seq", "head"),
        P("seq", "head", None),
        P("seq", "head", None),
        P("seq", "head"),
        P("head"),
        P("head"),
        P("head", "seq"),
        P(("seq", "head"), None),
        P(),
        P(),
        P("seq", "head"),
    )
    out_specs = (P(("seq", "head"), None), P("seq", "head"))
    return jax.shard_map(body, mesh=mesh, in_specs=in_specs, out_specs=out_specs, check_vma=False)
```

```python
import jax
import jax.numpy as jnp
from jax import lax
from jax.sharding import PartitionSpec as P

SPAN = 256


def shift_scan(decay, state, axis):
    devices = lax.axis_size(axis)

    def shifted(parts, distance):
        pairs = [(i, i + distance) for i in range(devices - distance)]
        a, s = parts
        return (
            lax.ppermute(a, axis, pairs),
            lax.ppermute(s.astype(jnp.bfloat16), axis, pairs).astype(jnp.float32),
        )

    acc = shifted((decay, state), 1)
    distance = 1
    while distance < devices:
        acc = carry_combine(shifted(acc, distance), acc)
        distance *= 2
    return acc


def carry_combine(earlier, later):
    decay_early, state_early = earlier
    decay_later, state_later = later
    return (
        decay_early + decay_later,
        jnp.exp(decay_later).reshape((-1,) + (1,) * (state_later.ndim - 1)) * state_early
        + state_later,
    )


def body(
    xin,
    gate_z,
    b_proj,
    c_proj,
    log_retain,
    skip_d,
    norm_gain,
    w_out,
    residual,
    refusal,
    stream_gain,
    w_in,
):
    seq_rows, channels = xin.shape
    head_count = log_retain.shape[1]
    head_width = channels // head_count
    group_count = b_proj.shape[1]
    state_width = b_proj.shape[2]
    per_group = head_count // group_count
    block_count = seq_rows // SPAN
    inputs = xin.reshape(block_count, SPAN, head_count, head_width)
    b_grouped = b_proj.reshape(block_count, SPAN, group_count, state_width)
    c_grouped = c_proj.reshape(block_count, SPAN, group_count, state_width)
    scores = jnp.einsum("klgn,ksgn->kgls", c_grouped, b_grouped, preferred_element_type=jnp.float32)
    scores = jnp.repeat(scores, per_group, axis=1)
    cum = jnp.cumsum(log_retain.reshape(block_count, SPAN, head_count), axis=1)
    cum_heads = jnp.transpose(cum, (0, 2, 1))
    later_pos = lax.broadcasted_iota(jnp.int32, (SPAN, SPAN), 0)
    earlier_pos = lax.broadcasted_iota(jnp.int32, (SPAN, SPAN), 1)
    causal = later_pos >= earlier_pos
    gap = cum_heads[:, :, :, None] - cum_heads[:, :, None, :]
    mixing = (jnp.where(causal, jnp.exp(jnp.where(causal, gap, 0.0)), 0.0) * scores).astype(
        jnp.bfloat16
    )
    intra = jnp.einsum("khls,kshp->klhp", mixing, inputs, preferred_element_type=jnp.float32)
    tail_decay = jnp.exp(cum_heads[:, :, -1:] - cum_heads)
    b_heads = jnp.repeat(b_grouped, per_group, axis=2)
    weighted_b = (
        b_heads.astype(jnp.float32) * jnp.transpose(tail_decay, (0, 2, 1))[..., None]
    ).astype(jnp.bfloat16)
    block_state = jnp.einsum(
        "klhn,klhp->khnp", weighted_b, inputs, preferred_element_type=jnp.float32
    )
    block_decay = cum_heads[:, :, -1]

    def advance(carried_state, pair):
        decay_here, state_here = pair
        return (jnp.exp(decay_here)[:, None, None] * carried_state + state_here, carried_state)

    zero_state = jnp.zeros((head_count, state_width, head_width), jnp.float32)
    device_state, local_starts = lax.scan(advance, zero_state, (block_decay, block_state))
    device_decay = jnp.sum(block_decay, axis=0)
    total_decay, incoming = shift_scan(
        device_decay, device_state.reshape(head_count, state_width * head_width), "seq"
    )
    incoming = incoming.reshape(head_count, state_width, head_width)
    before_block = jnp.cumsum(block_decay, axis=0) - block_decay
    starts = local_starts + jnp.exp(before_block)[:, :, None, None] * incoming[None]
    c_heads = jnp.repeat(c_grouped, per_group, axis=2).astype(jnp.float32)
    carried = jnp.einsum("klhn,khnp->klhp", c_heads, starts, precision=lax.Precision.HIGHEST)
    carried = carried * jnp.exp(cum)[..., None]
    mixed = intra + carried + skip_d[None, None, :, None] * inputs.astype(jnp.float32)
    gated = mixed * jax.nn.silu(
        gate_z.reshape(block_count, SPAN, head_count, head_width).astype(jnp.float32)
    )
    grouped = gated.reshape(seq_rows, group_count, per_group * head_width)
    grouped = grouped * lax.rsqrt(jnp.mean(grouped * grouped, axis=-1, keepdims=True) + 1e-05)
    ssd_out = (grouped.reshape(seq_rows, channels) * norm_gain[None, :]).astype(jnp.bfloat16)
    w_in_all = lax.all_gather(w_in, "seq", axis=0, tiled=True)
    ssd_out, w_in_all = lax.optimization_barrier((ssd_out, w_in_all))
    w_out_all = lax.all_gather(w_out, "seq", axis=1, tiled=True)
    unit = refusal / jnp.sqrt(jnp.sum(refusal * refusal) + 1e-06)
    head_devices = lax.axis_size("head")
    chunks = 2
    own_rows = residual.shape[0] // chunks
    ssd_parts = ssd_out.reshape(head_devices, chunks, own_rows, channels)
    streams, nexts = [], []
    for chunk in range(chunks):
        partial_sum = jnp.dot(
            ssd_parts[:, chunk].reshape(-1, channels),
            w_out_all,
            preferred_element_type=jnp.float32,
        )
        mixer_out = lax.psum_scatter(
            partial_sum.astype(jnp.bfloat16), "head", scatter_dimension=0, tiled=True
        ).astype(jnp.float32)
        rows = residual[chunk * own_rows:(chunk + 1) * own_rows]
        hidden = rows.astype(jnp.float32) + mixer_out
        coef = jnp.dot(hidden, unit, precision=lax.Precision.HIGHEST)
        stream = (hidden - coef[:, None] * unit[None, :]).astype(jnp.bfloat16)
        stream_float = stream.astype(jnp.float32)
        normed = (
            stream_float
            * lax.rsqrt(jnp.mean(stream_float * stream_float, axis=-1, keepdims=True) + 1e-05)
            * stream_gain[None, :]
        ).astype(jnp.bfloat16)
        all_rows = lax.all_gather(normed, "head", axis=0, tiled=True)
        next_part = jnp.dot(all_rows, w_in_all, preferred_element_type=jnp.float32)
        streams.append(stream)
        nexts.append(next_part.astype(jnp.bfloat16).reshape(head_devices, own_rows, -1))
    stream = jnp.concatenate(streams, axis=0)
    next_out = jnp.stack(nexts, axis=1).reshape(seq_rows, -1)
    return (stream, next_out)


def solution(mesh):
    in_specs = (
        P("seq", "head"),
        P("seq", "head"),
        P("seq", "head", None),
        P("seq", "head", None),
        P("seq", "head"),
        P("head"),
        P("head"),
        P("head", "seq"),
        P(("seq", "head"), None),
        P(),
        P(),
        P("seq", "head"),
    )
    out_specs = (P(("seq", "head"), None), P("seq", "head"))
    return jax.shard_map(body, mesh=mesh, in_specs=in_specs, out_specs=out_specs, check_vma=False)
```

```python
import jax
import jax.numpy as jnp
from jax import lax
from jax.sharding import PartitionSpec as P

SPAN = 256


def shift_scan(decay, state, axis):
    devices = lax.axis_size(axis)

    def shifted(parts, distance):
        pairs = [(i, i + distance) for i in range(devices - distance)]
        a, s = parts
        return (
            lax.ppermute(a, axis, pairs),
            lax.ppermute(s.astype(jnp.bfloat16), axis, pairs).astype(jnp.float32),
        )

    acc = shifted((decay, state), 1)
    distance = 1
    while distance < devices:
        acc = carry_combine(shifted(acc, distance), acc)
        distance *= 2
    return acc


def carry_combine(earlier, later):
    decay_early, state_early = earlier
    decay_later, state_later = later
    return (
        decay_early + decay_later,
        jnp.exp(decay_later).reshape((-1,) + (1,) * (state_later.ndim - 1)) * state_early
        + state_later,
    )


def body(
    xin,
    gate_z,
    b_proj,
    c_proj,
    log_retain,
    skip_d,
    norm_gain,
    w_out,
    residual,
    refusal,
    stream_gain,
    w_in,
):
    seq_rows, channels = xin.shape
    head_count = log_retain.shape[1]
    head_width = channels // head_count
    group_count = b_proj.shape[1]
    state_width = b_proj.shape[2]
    per_group = head_count // group_count
    block_count = seq_rows // SPAN
    inputs = xin.reshape(block_count, SPAN, head_count, head_width)
    b_grouped = b_proj.reshape(block_count, SPAN, group_count, state_width)
    c_grouped = c_proj.reshape(block_count, SPAN, group_count, state_width)
    scores = jnp.einsum("klgn,ksgn->kgls", c_grouped, b_grouped, preferred_element_type=jnp.float32)
    scores = jnp.repeat(scores, per_group, axis=1)
    cum = jnp.cumsum(log_retain.reshape(block_count, SPAN, head_count), axis=1)
    cum_heads = jnp.transpose(cum, (0, 2, 1))
    later_pos = lax.broadcasted_iota(jnp.int32, (SPAN, SPAN), 0)
    earlier_pos = lax.broadcasted_iota(jnp.int32, (SPAN, SPAN), 1)
    causal = later_pos >= earlier_pos
    gap = cum_heads[:, :, :, None] - cum_heads[:, :, None, :]
    mixing = (jnp.where(causal, jnp.exp(jnp.where(causal, gap, 0.0)), 0.0) * scores).astype(
        jnp.bfloat16
    )
    intra = jnp.einsum("khls,kshp->klhp", mixing, inputs, preferred_element_type=jnp.float32)
    tail_decay = jnp.exp(cum_heads[:, :, -1:] - cum_heads)
    b_heads = jnp.repeat(b_grouped, per_group, axis=2)
    weighted_b = (
        b_heads.astype(jnp.float32) * jnp.transpose(tail_decay, (0, 2, 1))[..., None]
    ).astype(jnp.bfloat16)
    block_state = jnp.einsum(
        "klhn,klhp->khnp", weighted_b, inputs, preferred_element_type=jnp.float32
    )
    block_decay = cum_heads[:, :, -1]

    def advance(carried_state, pair):
        decay_here, state_here = pair
        return (jnp.exp(decay_here)[:, None, None] * carried_state + state_here, carried_state)

    zero_state = jnp.zeros((head_count, state_width, head_width), jnp.float32)
    device_state, local_starts = lax.scan(advance, zero_state, (block_decay, block_state))
    device_decay = jnp.sum(block_decay, axis=0)
    total_decay, incoming = shift_scan(
        device_decay, device_state.reshape(head_count, state_width * head_width), "seq"
    )
    incoming = incoming.reshape(head_count, state_width, head_width)
    before_block = jnp.cumsum(block_decay, axis=0) - block_decay
    starts = local_starts + jnp.exp(before_block)[:, :, None, None] * incoming[None]
    c_heads = jnp.repeat(c_grouped, per_group, axis=2).astype(jnp.float32)
    carried = jnp.einsum("klhn,khnp->klhp", c_heads, starts, precision=lax.Precision.HIGHEST)
    carried = carried * jnp.exp(cum)[..., None]
    mixed = intra + carried + skip_d[None, None, :, None] * inputs.astype(jnp.float32)
    gated = mixed * jax.nn.silu(
        gate_z.reshape(block_count, SPAN, head_count, head_width).astype(jnp.float32)
    )
    grouped = gated.reshape(seq_rows, group_count, per_group * head_width)
    grouped = grouped * lax.rsqrt(jnp.mean(grouped * grouped, axis=-1, keepdims=True) + 1e-05)
    ssd_out = (grouped.reshape(seq_rows, channels) * norm_gain[None, :]).astype(jnp.bfloat16)
    both = lax.all_gather(jnp.stack([w_out.T, w_in]), "seq", axis=1, tiled=True)
    ssd_out, both = lax.optimization_barrier((ssd_out, both))
    w_in_all = both[1]
    partial_sum = lax.dot_general(
        ssd_out,
        both[0],
        (((1,), (1,)), ((), ())),
        preferred_element_type=jnp.float32,
    )
    mixer_out = lax.psum_scatter(
        partial_sum.astype(jnp.bfloat16), "head", scatter_dimension=0, tiled=True
    ).astype(jnp.float32)
    unit = refusal / jnp.sqrt(jnp.sum(refusal * refusal) + 1e-06)
    hidden = residual.astype(jnp.float32) + mixer_out
    coef = jnp.dot(hidden, unit, precision=lax.Precision.HIGHEST)
    stream = (hidden - coef[:, None] * unit[None, :]).astype(jnp.bfloat16)
    stream_float = stream.astype(jnp.float32)
    normed = (
        stream_float
        * lax.rsqrt(jnp.mean(stream_float * stream_float, axis=-1, keepdims=True) + 1e-05)
        * stream_gain[None, :]
    ).astype(jnp.bfloat16)
    all_rows = lax.all_gather(normed, "head", axis=0, tiled=True)
    next_float = jnp.dot(
        all_rows,
        w_in_all,
        preferred_element_type=jnp.float32,
    )
    return (stream, next_float.astype(jnp.bfloat16))


def solution(mesh):
    in_specs = (
        P("seq", "head"),
        P("seq", "head"),
        P("seq", "head", None),
        P("seq", "head", None),
        P("seq", "head"),
        P("head"),
        P("head"),
        P("head", "seq"),
        P(("seq", "head"), None),
        P(),
        P(),
        P("seq", "head"),
    )
    out_specs = (P(("seq", "head"), None), P("seq", "head"))
    return jax.shard_map(body, mesh=mesh, in_specs=in_specs, out_specs=out_specs, check_vma=False)
```

```python
import jax
import jax.numpy as jnp
from jax import lax
from jax.sharding import PartitionSpec as P

SPAN = 256


def shift_scan(decay, state, axis):
    devices = lax.axis_size(axis)

    def shifted(parts, distance):
        pairs = [(i, i + distance) for i in range(devices - distance)]
        a, s = parts
        return (
            lax.ppermute(a, axis, pairs),
            lax.ppermute(s.astype(jnp.bfloat16), axis, pairs).astype(jnp.float32),
        )

    acc = shifted((decay, state), 1)
    distance = 1
    while distance < devices:
        acc = carry_combine(shifted(acc, distance), acc)
        distance *= 2
    return acc


def carry_combine(earlier, later):
    decay_early, state_early = earlier
    decay_later, state_later = later
    return (
        decay_early + decay_later,
        jnp.exp(decay_later).reshape((-1,) + (1,) * (state_later.ndim - 1)) * state_early
        + state_later,
    )


def body(
    xin,
    gate_z,
    b_proj,
    c_proj,
    log_retain,
    skip_d,
    norm_gain,
    w_out,
    residual,
    refusal,
    stream_gain,
    w_in,
):
    seq_rows, channels = xin.shape
    head_count = log_retain.shape[1]
    head_width = channels // head_count
    group_count = b_proj.shape[1]
    state_width = b_proj.shape[2]
    per_group = head_count // group_count
    block_count = seq_rows // SPAN
    inputs = xin.reshape(block_count, SPAN, head_count, head_width)
    b_grouped = b_proj.reshape(block_count, SPAN, group_count, state_width)
    c_grouped = c_proj.reshape(block_count, SPAN, group_count, state_width)
    scores = jnp.einsum("klgn,ksgn->kgls", c_grouped, b_grouped, preferred_element_type=jnp.float32)
    scores = jnp.repeat(scores, per_group, axis=1)
    cum = jnp.cumsum(log_retain.reshape(block_count, SPAN, head_count), axis=1)
    cum_heads = jnp.transpose(cum, (0, 2, 1))
    later_pos = lax.broadcasted_iota(jnp.int32, (SPAN, SPAN), 0)
    earlier_pos = lax.broadcasted_iota(jnp.int32, (SPAN, SPAN), 1)
    causal = later_pos >= earlier_pos
    gap = cum_heads[:, :, :, None] - cum_heads[:, :, None, :]
    mixing = (jnp.where(causal, jnp.exp(jnp.where(causal, gap, 0.0)), 0.0) * scores).astype(
        jnp.bfloat16
    )
    intra = jnp.einsum("khls,kshp->klhp", mixing, inputs, preferred_element_type=jnp.float32)
    tail_decay = jnp.exp(cum_heads[:, :, -1:] - cum_heads)
    b_heads = jnp.repeat(b_grouped, per_group, axis=2)
    weighted_b = (
        b_heads.astype(jnp.float32) * jnp.transpose(tail_decay, (0, 2, 1))[..., None]
    ).astype(jnp.bfloat16)
    block_state = jnp.einsum(
        "klhn,klhp->khnp", weighted_b, inputs, preferred_element_type=jnp.float32
    )
    block_decay = cum_heads[:, :, -1]

    def advance(carried_state, pair):
        decay_here, state_here = pair
        return (jnp.exp(decay_here)[:, None, None] * carried_state + state_here, carried_state)

    zero_state = jnp.zeros((head_count, state_width, head_width), jnp.float32)
    device_state, local_starts = lax.scan(advance, zero_state, (block_decay, block_state))
    device_decay = jnp.sum(block_decay, axis=0)
    w_out_all = lax.all_gather(w_out, "seq", axis=1, tiled=True)
    w_in_late, device_state = lax.optimization_barrier((w_in, device_state))
    w_in_all = lax.all_gather(w_in_late, "seq", axis=0, tiled=True)
    total_decay, incoming = shift_scan(
        device_decay, device_state.reshape(head_count, state_width * head_width), "seq"
    )
    incoming = incoming.reshape(head_count, state_width, head_width)
    before_block = jnp.cumsum(block_decay, axis=0) - block_decay
    starts = local_starts + jnp.exp(before_block)[:, :, None, None] * incoming[None]
    c_heads = jnp.repeat(c_grouped, per_group, axis=2).astype(jnp.float32)
    carried = jnp.einsum("klhn,khnp->klhp", c_heads, starts, precision=lax.Precision.HIGHEST)
    carried = carried * jnp.exp(cum)[..., None]
    mixed = intra + carried + skip_d[None, None, :, None] * inputs.astype(jnp.float32)
    gated = mixed * jax.nn.silu(
        gate_z.reshape(block_count, SPAN, head_count, head_width).astype(jnp.float32)
    )
    grouped = gated.reshape(seq_rows, group_count, per_group * head_width)
    grouped = grouped * lax.rsqrt(jnp.mean(grouped * grouped, axis=-1, keepdims=True) + 1e-05)
    ssd_out = (grouped.reshape(seq_rows, channels) * norm_gain[None, :]).astype(jnp.bfloat16)
    partial_sum = jnp.dot(
        ssd_out,
        w_out_all,
        preferred_element_type=jnp.float32,
    ).astype(jnp.bfloat16)
    partial_sum, w_in_all = lax.optimization_barrier((partial_sum, w_in_all))
    mixer_out = lax.psum_scatter(
        partial_sum, "head", scatter_dimension=0, tiled=True
    ).astype(jnp.float32)
    unit = refusal / jnp.sqrt(jnp.sum(refusal * refusal) + 1e-06)
    hidden = residual.astype(jnp.float32) + mixer_out
    coef = jnp.dot(hidden, unit, precision=lax.Precision.HIGHEST)
    stream = (hidden - coef[:, None] * unit[None, :]).astype(jnp.bfloat16)
    stream_float = stream.astype(jnp.float32)
    normed = (
        stream_float
        * lax.rsqrt(jnp.mean(stream_float * stream_float, axis=-1, keepdims=True) + 1e-05)
        * stream_gain[None, :]
    ).astype(jnp.bfloat16)
    all_rows = lax.all_gather(normed, "head", axis=0, tiled=True)
    next_float = jnp.dot(
        all_rows,
        w_in_all,
        preferred_element_type=jnp.float32,
    )
    return (stream, next_float.astype(jnp.bfloat16))


def solution(mesh):
    in_specs = (
        P("seq", "head"),
        P("seq", "head"),
        P("seq", "head", None),
        P("seq", "head", None),
        P("seq", "head"),
        P("head"),
        P("head"),
        P("head", "seq"),
        P(("seq", "head"), None),
        P(),
        P(),
        P("seq", "head"),
    )
    out_specs = (P(("seq", "head"), None), P("seq", "head"))
    return jax.shard_map(body, mesh=mesh, in_specs=in_specs, out_specs=out_specs, check_vma=False)
```

```python
import jax
import jax.numpy as jnp
from jax import lax
from jax.sharding import PartitionSpec as P

SPAN = 256


def shift_scan(decay, state, axis):
    devices = lax.axis_size(axis)

    def shifted(parts, distance):
        pairs = [(i, i + distance) for i in range(devices - distance)]
        a, s = parts
        return (
            lax.ppermute(a, axis, pairs),
            lax.ppermute(s.astype(jnp.bfloat16), axis, pairs).astype(jnp.float32),
        )

    acc = shifted((decay, state), 1)
    distance = 1
    while distance < devices:
        acc = carry_combine(shifted(acc, distance), acc)
        distance *= 2
    return acc


def carry_combine(earlier, later):
    decay_early, state_early = earlier
    decay_later, state_later = later
    return (
        decay_early + decay_later,
        jnp.exp(decay_later).reshape((-1,) + (1,) * (state_later.ndim - 1)) * state_early
        + state_later,
    )


def body(
    xin,
    gate_z,
    b_proj,
    c_proj,
    log_retain,
    skip_d,
    norm_gain,
    w_out,
    residual,
    refusal,
    stream_gain,
    w_in,
):
    seq_rows, channels = xin.shape
    head_count = log_retain.shape[1]
    head_width = channels // head_count
    group_count = b_proj.shape[1]
    state_width = b_proj.shape[2]
    per_group = head_count // group_count
    block_count = seq_rows // SPAN
    inputs = xin.reshape(block_count, SPAN, head_count, head_width)
    b_grouped = b_proj.reshape(block_count, SPAN, group_count, state_width)
    c_grouped = c_proj.reshape(block_count, SPAN, group_count, state_width)
    scores = jnp.einsum("klgn,ksgn->kgls", c_grouped, b_grouped, preferred_element_type=jnp.float32)
    scores = jnp.repeat(scores, per_group, axis=1)
    cum = jnp.cumsum(log_retain.reshape(block_count, SPAN, head_count), axis=1)
    cum_heads = jnp.transpose(cum, (0, 2, 1))
    later_pos = lax.broadcasted_iota(jnp.int32, (SPAN, SPAN), 0)
    earlier_pos = lax.broadcasted_iota(jnp.int32, (SPAN, SPAN), 1)
    causal = later_pos >= earlier_pos
    gap = cum_heads[:, :, :, None] - cum_heads[:, :, None, :]
    mixing = (jnp.where(causal, jnp.exp(jnp.where(causal, gap, 0.0)), 0.0) * scores).astype(
        jnp.bfloat16
    )
    intra = jnp.einsum("khls,kshp->klhp", mixing, inputs, preferred_element_type=jnp.float32)
    tail_decay = jnp.exp(cum_heads[:, :, -1:] - cum_heads)
    b_heads = jnp.repeat(b_grouped, per_group, axis=2)
    weighted_b = (
        b_heads.astype(jnp.float32) * jnp.transpose(tail_decay, (0, 2, 1))[..., None]
    ).astype(jnp.bfloat16)
    block_state = jnp.einsum(
        "klhn,klhp->khnp", weighted_b, inputs, preferred_element_type=jnp.float32
    )
    block_decay = cum_heads[:, :, -1]

    def advance(carried_state, pair):
        decay_here, state_here = pair
        return (jnp.exp(decay_here)[:, None, None] * carried_state + state_here, carried_state)

    zero_state = jnp.zeros((head_count, state_width, head_width), jnp.float32)
    device_state, local_starts = lax.scan(advance, zero_state, (block_decay, block_state))
    device_decay = jnp.sum(block_decay, axis=0)
    total_decay, incoming = shift_scan(
        device_decay, device_state.reshape(head_count, state_width * head_width), "seq"
    )
    incoming = incoming.reshape(head_count, state_width, head_width)
    before_block = jnp.cumsum(block_decay, axis=0) - block_decay
    starts = local_starts + jnp.exp(before_block)[:, :, None, None] * incoming[None]
    c_heads = jnp.repeat(c_grouped, per_group, axis=2).astype(jnp.float32)
    carried = jnp.einsum("klhn,khnp->klhp", c_heads, starts, precision=lax.Precision.HIGHEST)
    carried = carried * jnp.exp(cum)[..., None]
    mixed = intra + carried + skip_d[None, None, :, None] * inputs.astype(jnp.float32)
    gated = mixed * jax.nn.silu(
        gate_z.reshape(block_count, SPAN, head_count, head_width).astype(jnp.float32)
    )
    grouped = gated.reshape(seq_rows, group_count, per_group * head_width)
    grouped = grouped * lax.rsqrt(jnp.mean(grouped * grouped, axis=-1, keepdims=True) + 1e-05)
    ssd_out = (grouped.reshape(seq_rows, channels) * norm_gain[None, :]).astype(jnp.bfloat16)
    w_in_all = lax.all_gather(w_in, "seq", axis=0, tiled=True)
    ssd_out, w_in_all = lax.optimization_barrier((ssd_out, w_in_all))
    partial_sum = jnp.dot(
        ssd_out,
        lax.all_gather(w_out, "seq", axis=1, tiled=True),
        preferred_element_type=jnp.float32,
    )
    own_rows = residual.shape[0]
    mine = lax.axis_index("head")
    with_residual = lax.dynamic_update_slice_in_dim(
        partial_sum,
        lax.dynamic_slice_in_dim(partial_sum, mine * own_rows, own_rows)
        + residual.astype(jnp.float32),
        mine * own_rows,
        axis=0,
    )
    hidden = lax.psum(with_residual.astype(jnp.bfloat16), "head").astype(jnp.float32)
    unit = refusal / jnp.sqrt(jnp.sum(refusal * refusal) + 1e-06)
    coef = jnp.dot(hidden, unit, precision=lax.Precision.HIGHEST)
    stream_all = (hidden - coef[:, None] * unit[None, :]).astype(jnp.bfloat16)
    stream_float = stream_all.astype(jnp.float32)
    all_rows = (
        stream_float
        * lax.rsqrt(jnp.mean(stream_float * stream_float, axis=-1, keepdims=True) + 1e-05)
        * stream_gain[None, :]
    ).astype(jnp.bfloat16)
    stream = lax.dynamic_slice_in_dim(stream_all, mine * own_rows, own_rows)
    next_float = jnp.dot(
        all_rows,
        w_in_all,
        preferred_element_type=jnp.float32,
    )
    return (stream, next_float.astype(jnp.bfloat16))


def solution(mesh):
    in_specs = (
        P("seq", "head"),
        P("seq", "head"),
        P("seq", "head", None),
        P("seq", "head", None),
        P("seq", "head"),
        P("head"),
        P("head"),
        P("head", "seq"),
        P(("seq", "head"), None),
        P(),
        P(),
        P("seq", "head"),
    )
    out_specs = (P(("seq", "head"), None), P("seq", "head"))
    return jax.shard_map(body, mesh=mesh, in_specs=in_specs, out_specs=out_specs, check_vma=False)
```

```python
import jax
import jax.numpy as jnp
from jax import lax
from jax.sharding import PartitionSpec as P

SPAN = 256


def shift_scan(decay, state, axis):
    devices = lax.axis_size(axis)

    def shifted(parts, distance):
        pairs = [(i, i + distance) for i in range(devices - distance)]
        a, s = parts
        return (
            lax.ppermute(a, axis, pairs),
            lax.ppermute(s.astype(jnp.bfloat16), axis, pairs).astype(jnp.float32),
        )

    acc = shifted((decay, state), 1)
    distance = 1
    while distance < devices:
        acc = carry_combine(shifted(acc, distance), acc)
        distance *= 2
    return acc


def carry_combine(earlier, later):
    decay_early, state_early = earlier
    decay_later, state_later = later
    return (
        decay_early + decay_later,
        jnp.exp(decay_later).reshape((-1,) + (1,) * (state_later.ndim - 1)) * state_early
        + state_later,
    )


def body(
    xin,
    gate_z,
    b_proj,
    c_proj,
    log_retain,
    skip_d,
    norm_gain,
    w_out,
    residual,
    refusal,
    stream_gain,
    w_in,
):
    seq_rows, channels = xin.shape
    head_count = log_retain.shape[1]
    head_width = channels // head_count
    group_count = b_proj.shape[1]
    state_width = b_proj.shape[2]
    per_group = head_count // group_count
    block_count = seq_rows // SPAN
    inputs = xin.reshape(block_count, SPAN, head_count, head_width)
    b_grouped = b_proj.reshape(block_count, SPAN, group_count, state_width)
    c_grouped = c_proj.reshape(block_count, SPAN, group_count, state_width)
    scores = jnp.einsum("klgn,ksgn->kgls", c_grouped, b_grouped, preferred_element_type=jnp.float32)
    scores = jnp.repeat(scores, per_group, axis=1)
    cum = jnp.cumsum(log_retain.reshape(block_count, SPAN, head_count), axis=1)
    cum_heads = jnp.transpose(cum, (0, 2, 1))
    later_pos = lax.broadcasted_iota(jnp.int32, (SPAN, SPAN), 0)
    earlier_pos = lax.broadcasted_iota(jnp.int32, (SPAN, SPAN), 1)
    causal = later_pos >= earlier_pos
    gap = cum_heads[:, :, :, None] - cum_heads[:, :, None, :]
    mixing = (jnp.where(causal, jnp.exp(jnp.where(causal, gap, 0.0)), 0.0) * scores).astype(
        jnp.bfloat16
    )
    intra = jnp.einsum("khls,kshp->klhp", mixing, inputs, preferred_element_type=jnp.float32)
    tail_decay = jnp.exp(cum_heads[:, :, -1:] - cum_heads)
    b_heads = jnp.repeat(b_grouped, per_group, axis=2)
    weighted_b = (
        b_heads.astype(jnp.float32) * jnp.transpose(tail_decay, (0, 2, 1))[..., None]
    ).astype(jnp.bfloat16)
    block_state = jnp.einsum(
        "klhn,klhp->khnp", weighted_b, inputs, preferred_element_type=jnp.float32
    )
    block_decay = cum_heads[:, :, -1]

    device_state = jnp.zeros((head_count, state_width, head_width), jnp.float32)
    starts_list = []
    for block in range(block_count):
        starts_list.append(device_state)
        device_state = (
            jnp.exp(block_decay[block])[:, None, None] * device_state + block_state[block]
        )
    local_starts = jnp.stack(starts_list)
    device_decay = jnp.sum(block_decay, axis=0)
    total_decay, incoming = shift_scan(
        device_decay, device_state.reshape(head_count, state_width * head_width), "seq"
    )
    incoming = incoming.reshape(head_count, state_width, head_width)
    before_block = jnp.cumsum(block_decay, axis=0) - block_decay
    starts = local_starts + jnp.exp(before_block)[:, :, None, None] * incoming[None]
    c_heads = jnp.repeat(c_grouped, per_group, axis=2).astype(jnp.float32)
    carried = jnp.einsum("klhn,khnp->klhp", c_heads, starts, precision=lax.Precision.HIGHEST)
    carried = carried * jnp.exp(cum)[..., None]
    mixed = intra + carried + skip_d[None, None, :, None] * inputs.astype(jnp.float32)
    gated = mixed * jax.nn.silu(
        gate_z.reshape(block_count, SPAN, head_count, head_width).astype(jnp.float32)
    )
    grouped = gated.reshape(seq_rows, group_count, per_group * head_width)
    grouped = grouped * lax.rsqrt(jnp.mean(grouped * grouped, axis=-1, keepdims=True) + 1e-05)
    ssd_out = (grouped.reshape(seq_rows, channels) * norm_gain[None, :]).astype(jnp.bfloat16)
    w_in_all = lax.all_gather(w_in, "seq", axis=0, tiled=True)
    ssd_out, w_in_all = lax.optimization_barrier((ssd_out, w_in_all))
    own_rows = residual.shape[0]
    mine = lax.axis_index("head")
    residual_rows = lax.dynamic_update_slice_in_dim(
        jnp.zeros((seq_rows, residual.shape[1]), jnp.float32),
        residual.astype(jnp.float32),
        mine * own_rows,
        axis=0,
    )
    partial_sum = jnp.dot(
        ssd_out,
        lax.all_gather(w_out, "seq", axis=1, tiled=True),
        preferred_element_type=jnp.float32,
    )
    with_residual = (partial_sum + residual_rows).astype(jnp.bfloat16)
    hidden = lax.psum(with_residual, "head").astype(jnp.float32)
    unit = refusal / jnp.sqrt(jnp.sum(refusal * refusal) + 1e-06)
    coef = jnp.dot(hidden, unit, precision=lax.Precision.HIGHEST)
    stream_all = (hidden - coef[:, None] * unit[None, :]).astype(jnp.bfloat16)
    stream_float = stream_all.astype(jnp.float32)
    all_rows = (
        stream_float
        * lax.rsqrt(jnp.mean(stream_float * stream_float, axis=-1, keepdims=True) + 1e-05)
        * stream_gain[None, :]
    ).astype(jnp.bfloat16)
    stream = lax.dynamic_slice_in_dim(stream_all, mine * own_rows, own_rows)
    next_float = jnp.dot(
        all_rows,
        w_in_all,
        preferred_element_type=jnp.float32,
    )
    return (stream, next_float.astype(jnp.bfloat16))


def solution(mesh):
    in_specs = (
        P("seq", "head"),
        P("seq", "head"),
        P("seq", "head", None),
        P("seq", "head", None),
        P("seq", "head"),
        P("head"),
        P("head"),
        P("head", "seq"),
        P(("seq", "head"), None),
        P(),
        P(),
        P("seq", "head"),
    )
    out_specs = (P(("seq", "head"), None), P("seq", "head"))
    return jax.shard_map(body, mesh=mesh, in_specs=in_specs, out_specs=out_specs, check_vma=False)
```

```python
import jax
import jax.numpy as jnp
from jax import lax
from jax.sharding import PartitionSpec as P

SPAN = 256


def shift_scan(decay, state, axis):
    devices = lax.axis_size(axis)

    def shifted(parts, distance):
        pairs = [(i, i + distance) for i in range(devices - distance)]
        a, s = parts
        high = a.astype(jnp.bfloat16)
        low = (a - high.astype(jnp.float32)).astype(jnp.bfloat16)
        tail = jnp.zeros((s.shape[0], 128), jnp.bfloat16)
        tail = tail.at[:, 0].set(high).at[:, 1].set(low)
        packed = jnp.concatenate([s.astype(jnp.bfloat16), tail], axis=1)
        got = lax.ppermute(packed, axis, pairs)
        width = s.shape[1]
        return (
            got[:, width].astype(jnp.float32) + got[:, width + 1].astype(jnp.float32),
            got[:, :width].astype(jnp.float32),
        )

    acc = shifted((decay, state), 1)
    distance = 1
    while distance < devices:
        acc = carry_combine(shifted(acc, distance), acc)
        distance *= 2
    return acc


def carry_combine(earlier, later):
    decay_early, state_early = earlier
    decay_later, state_later = later
    return (
        decay_early + decay_later,
        jnp.exp(decay_later).reshape((-1,) + (1,) * (state_later.ndim - 1)) * state_early
        + state_later,
    )


def body(
    xin,
    gate_z,
    b_proj,
    c_proj,
    log_retain,
    skip_d,
    norm_gain,
    w_out,
    residual,
    refusal,
    stream_gain,
    w_in,
):
    seq_rows, channels = xin.shape
    head_count = log_retain.shape[1]
    head_width = channels // head_count
    group_count = b_proj.shape[1]
    state_width = b_proj.shape[2]
    per_group = head_count // group_count
    block_count = seq_rows // SPAN
    inputs = xin.reshape(block_count, SPAN, head_count, head_width)
    b_grouped = b_proj.reshape(block_count, SPAN, group_count, state_width)
    c_grouped = c_proj.reshape(block_count, SPAN, group_count, state_width)
    scores = jnp.einsum("klgn,ksgn->kgls", c_grouped, b_grouped, preferred_element_type=jnp.float32)
    scores = jnp.repeat(scores, per_group, axis=1)
    cum = jnp.cumsum(log_retain.reshape(block_count, SPAN, head_count), axis=1)
    cum_heads = jnp.transpose(cum, (0, 2, 1))
    later_pos = lax.broadcasted_iota(jnp.int32, (SPAN, SPAN), 0)
    earlier_pos = lax.broadcasted_iota(jnp.int32, (SPAN, SPAN), 1)
    causal = later_pos >= earlier_pos
    gap = cum_heads[:, :, :, None] - cum_heads[:, :, None, :]
    mixing = (jnp.where(causal, jnp.exp(jnp.where(causal, gap, 0.0)), 0.0) * scores).astype(
        jnp.bfloat16
    )
    intra = jnp.einsum("khls,kshp->klhp", mixing, inputs, preferred_element_type=jnp.float32)
    tail_decay = jnp.exp(cum_heads[:, :, -1:] - cum_heads)
    b_heads = jnp.repeat(b_grouped, per_group, axis=2)
    weighted_b = (
        b_heads.astype(jnp.float32) * jnp.transpose(tail_decay, (0, 2, 1))[..., None]
    ).astype(jnp.bfloat16)
    block_state = jnp.einsum(
        "klhn,klhp->khnp", weighted_b, inputs, preferred_element_type=jnp.float32
    )
    block_decay = cum_heads[:, :, -1]

    device_state = jnp.zeros((head_count, state_width, head_width), jnp.float32)
    starts_list = []
    for block in range(block_count):
        starts_list.append(device_state)
        device_state = (
            jnp.exp(block_decay[block])[:, None, None] * device_state + block_state[block]
        )
    local_starts = jnp.stack(starts_list)
    device_decay = jnp.sum(block_decay, axis=0)
    total_decay, incoming = shift_scan(
        device_decay, device_state.reshape(head_count, state_width * head_width), "seq"
    )
    incoming = incoming.reshape(head_count, state_width, head_width)
    before_block = jnp.cumsum(block_decay, axis=0) - block_decay
    starts = local_starts + jnp.exp(before_block)[:, :, None, None] * incoming[None]
    c_heads = jnp.repeat(c_grouped, per_group, axis=2).astype(jnp.float32)
    carried = jnp.einsum("klhn,khnp->klhp", c_heads, starts, precision=lax.Precision.HIGHEST)
    carried = carried * jnp.exp(cum)[..., None]
    mixed = intra + carried + skip_d[None, None, :, None] * inputs.astype(jnp.float32)
    gated = mixed * jax.nn.silu(
        gate_z.reshape(block_count, SPAN, head_count, head_width).astype(jnp.float32)
    )
    grouped = gated.reshape(seq_rows, group_count, per_group * head_width)
    grouped = grouped * lax.rsqrt(jnp.mean(grouped * grouped, axis=-1, keepdims=True) + 1e-05)
    ssd_out = (grouped.reshape(seq_rows, channels) * norm_gain[None, :]).astype(jnp.bfloat16)
    w_in_all = lax.all_gather(w_in, "seq", axis=0, tiled=True)
    ssd_out, w_in_all = lax.optimization_barrier((ssd_out, w_in_all))
    own_rows = residual.shape[0]
    mine = lax.axis_index("head")
    residual_rows = lax.dynamic_update_slice_in_dim(
        jnp.zeros((seq_rows, residual.shape[1]), jnp.float32),
        residual.astype(jnp.float32),
        mine * own_rows,
        axis=0,
    )
    partial_sum = jnp.dot(
        ssd_out,
        lax.all_gather(w_out, "seq", axis=1, tiled=True),
        preferred_element_type=jnp.float32,
    )
    with_residual = (partial_sum + residual_rows).astype(jnp.bfloat16)
    hidden = lax.psum(with_residual, "head").astype(jnp.float32)
    unit = refusal / jnp.sqrt(jnp.sum(refusal * refusal) + 1e-06)
    coef = jnp.dot(hidden, unit, precision=lax.Precision.HIGHEST)
    stream_all = (hidden - coef[:, None] * unit[None, :]).astype(jnp.bfloat16)
    stream_float = stream_all.astype(jnp.float32)
    all_rows = (
        stream_float
        * lax.rsqrt(jnp.mean(stream_float * stream_float, axis=-1, keepdims=True) + 1e-05)
        * stream_gain[None, :]
    ).astype(jnp.bfloat16)
    stream = lax.dynamic_slice_in_dim(stream_all, mine * own_rows, own_rows)
    next_float = jnp.dot(
        all_rows,
        w_in_all,
        preferred_element_type=jnp.float32,
    )
    return (stream, next_float.astype(jnp.bfloat16))


def solution(mesh):
    in_specs = (
        P("seq", "head"),
        P("seq", "head"),
        P("seq", "head", None),
        P("seq", "head", None),
        P("seq", "head"),
        P("head"),
        P("head"),
        P("head", "seq"),
        P(("seq", "head"), None),
        P(),
        P(),
        P("seq", "head"),
    )
    out_specs = (P(("seq", "head"), None), P("seq", "head"))
    return jax.shard_map(body, mesh=mesh, in_specs=in_specs, out_specs=out_specs, check_vma=False)
```

```python
import jax
import jax.numpy as jnp
from jax import lax
from jax.sharding import PartitionSpec as P

SPAN = 256


def shift_scan(decay, state, axis):
    devices = lax.axis_size(axis)

    def shifted(parts, distance):
        pairs = [(i, i + distance) for i in range(devices - distance)]
        a, s = parts
        return (
            lax.ppermute(a, axis, pairs),
            lax.ppermute(s.astype(jnp.bfloat16), axis, pairs).astype(jnp.float32),
        )

    acc = shifted((decay, state), 1)
    distance = 1
    while distance < devices:
        acc = carry_combine(shifted(acc, distance), acc)
        distance *= 2
    return acc


def carry_combine(earlier, later):
    decay_early, state_early = earlier
    decay_later, state_later = later
    return (
        decay_early + decay_later,
        jnp.exp(decay_later).reshape((-1,) + (1,) * (state_later.ndim - 1)) * state_early
        + state_later,
    )


def body(
    xin,
    gate_z,
    b_proj,
    c_proj,
    log_retain,
    skip_d,
    norm_gain,
    w_out,
    residual,
    refusal,
    stream_gain,
    w_in,
):
    seq_rows, channels = xin.shape
    head_count = log_retain.shape[1]
    head_width = channels // head_count
    group_count = b_proj.shape[1]
    state_width = b_proj.shape[2]
    per_group = head_count // group_count
    block_count = seq_rows // SPAN
    inputs = xin.reshape(block_count, SPAN, head_count, head_width)
    b_grouped = b_proj.reshape(block_count, SPAN, group_count, state_width)
    c_grouped = c_proj.reshape(block_count, SPAN, group_count, state_width)
    scores = jnp.einsum("klgn,ksgn->kgls", c_grouped, b_grouped, preferred_element_type=jnp.float32)
    scores = jnp.repeat(scores, per_group, axis=1)
    cum = jnp.cumsum(log_retain.reshape(block_count, SPAN, head_count), axis=1)
    w_out_all = lax.all_gather(w_out, "seq", axis=1, tiled=True)
    w_in_early, cum = lax.optimization_barrier((w_in, cum))
    w_in_all = lax.all_gather(w_in_early, "seq", axis=0, tiled=True)
    cum_heads = jnp.transpose(cum, (0, 2, 1))
    later_pos = lax.broadcasted_iota(jnp.int32, (SPAN, SPAN), 0)
    earlier_pos = lax.broadcasted_iota(jnp.int32, (SPAN, SPAN), 1)
    causal = later_pos >= earlier_pos
    gap = cum_heads[:, :, :, None] - cum_heads[:, :, None, :]
    mixing = (jnp.where(causal, jnp.exp(jnp.where(causal, gap, 0.0)), 0.0) * scores).astype(
        jnp.bfloat16
    )
    intra = jnp.einsum("khls,kshp->klhp", mixing, inputs, preferred_element_type=jnp.float32)
    tail_decay = jnp.exp(cum_heads[:, :, -1:] - cum_heads)
    b_heads = jnp.repeat(b_grouped, per_group, axis=2)
    weighted_b = (
        b_heads.astype(jnp.float32) * jnp.transpose(tail_decay, (0, 2, 1))[..., None]
    ).astype(jnp.bfloat16)
    block_state = jnp.einsum(
        "klhn,klhp->khnp", weighted_b, inputs, preferred_element_type=jnp.float32
    )
    block_decay = cum_heads[:, :, -1]

    device_state = jnp.zeros((head_count, state_width, head_width), jnp.float32)
    starts_list = []
    for block in range(block_count):
        starts_list.append(device_state)
        device_state = (
            jnp.exp(block_decay[block])[:, None, None] * device_state + block_state[block]
        )
    local_starts = jnp.stack(starts_list)
    device_decay = jnp.sum(block_decay, axis=0)
    total_decay, incoming = shift_scan(
        device_decay, device_state.reshape(head_count, state_width * head_width), "seq"
    )
    incoming = incoming.reshape(head_count, state_width, head_width)
    before_block = jnp.cumsum(block_decay, axis=0) - block_decay
    starts = local_starts + jnp.exp(before_block)[:, :, None, None] * incoming[None]
    c_heads = jnp.repeat(c_grouped, per_group, axis=2).astype(jnp.float32)
    carried = jnp.einsum("klhn,khnp->klhp", c_heads, starts, precision=lax.Precision.HIGHEST)
    carried = carried * jnp.exp(cum)[..., None]
    mixed = intra + carried + skip_d[None, None, :, None] * inputs.astype(jnp.float32)
    gated = mixed * jax.nn.silu(
        gate_z.reshape(block_count, SPAN, head_count, head_width).astype(jnp.float32)
    )
    grouped = gated.reshape(seq_rows, group_count, per_group * head_width)
    grouped = grouped * lax.rsqrt(jnp.mean(grouped * grouped, axis=-1, keepdims=True) + 1e-05)
    ssd_out = (grouped.reshape(seq_rows, channels) * norm_gain[None, :]).astype(jnp.bfloat16)
    own_rows = residual.shape[0]
    mine = lax.axis_index("head")
    residual_rows = lax.dynamic_update_slice_in_dim(
        jnp.zeros((seq_rows, residual.shape[1]), jnp.float32),
        residual.astype(jnp.float32),
        mine * own_rows,
        axis=0,
    )
    partial_sum = jnp.dot(
        ssd_out,
        w_out_all,
        preferred_element_type=jnp.float32,
    )
    with_residual = (partial_sum + residual_rows).astype(jnp.bfloat16)
    with_residual, w_in_all = lax.optimization_barrier((with_residual, w_in_all))
    hidden = lax.psum(with_residual, "head").astype(jnp.float32)
    unit = refusal / jnp.sqrt(jnp.sum(refusal * refusal) + 1e-06)
    coef = jnp.dot(hidden, unit, precision=lax.Precision.HIGHEST)
    stream_all = (hidden - coef[:, None] * unit[None, :]).astype(jnp.bfloat16)
    stream_float = stream_all.astype(jnp.float32)
    all_rows = (
        stream_float
        * lax.rsqrt(jnp.mean(stream_float * stream_float, axis=-1, keepdims=True) + 1e-05)
        * stream_gain[None, :]
    ).astype(jnp.bfloat16)
    stream = lax.dynamic_slice_in_dim(stream_all, mine * own_rows, own_rows)
    next_float = jnp.dot(
        all_rows,
        w_in_all,
        preferred_element_type=jnp.float32,
    )
    return (stream, next_float.astype(jnp.bfloat16))


def solution(mesh):
    in_specs = (
        P("seq", "head"),
        P("seq", "head"),
        P("seq", "head", None),
        P("seq", "head", None),
        P("seq", "head"),
        P("head"),
        P("head"),
        P("head", "seq"),
        P(("seq", "head"), None),
        P(),
        P(),
        P("seq", "head"),
    )
    out_specs = (P(("seq", "head"), None), P("seq", "head"))
    return jax.shard_map(body, mesh=mesh, in_specs=in_specs, out_specs=out_specs, check_vma=False)
```

```python
import jax
import jax.numpy as jnp
from jax import lax
from jax.sharding import PartitionSpec as P

SPAN = 256


def shift_scan(decay, state, axis):
    devices = lax.axis_size(axis)

    def shifted(parts, distance):
        pairs = [(i, i + distance) for i in range(devices - distance)]
        a, s = parts
        return (
            lax.ppermute(a, axis, pairs),
            lax.ppermute(s.astype(jnp.bfloat16), axis, pairs).astype(jnp.float32),
        )

    acc = shifted((decay, state), 1)
    distance = 1
    if devices > 2:
        acc = carry_combine(shifted((decay, state), 2), acc)
        distance = 2
    while distance < devices:
        acc = carry_combine(shifted(acc, distance), acc)
        distance *= 2
    return acc


def carry_combine(earlier, later):
    decay_early, state_early = earlier
    decay_later, state_later = later
    return (
        decay_early + decay_later,
        jnp.exp(decay_later).reshape((-1,) + (1,) * (state_later.ndim - 1)) * state_early
        + state_later,
    )


def body(
    xin,
    gate_z,
    b_proj,
    c_proj,
    log_retain,
    skip_d,
    norm_gain,
    w_out,
    residual,
    refusal,
    stream_gain,
    w_in,
):
    seq_rows, channels = xin.shape
    head_count = log_retain.shape[1]
    head_width = channels // head_count
    group_count = b_proj.shape[1]
    state_width = b_proj.shape[2]
    per_group = head_count // group_count
    block_count = seq_rows // SPAN
    inputs = xin.reshape(block_count, SPAN, head_count, head_width)
    b_grouped = b_proj.reshape(block_count, SPAN, group_count, state_width)
    c_grouped = c_proj.reshape(block_count, SPAN, group_count, state_width)
    scores = jnp.einsum("klgn,ksgn->kgls", c_grouped, b_grouped, preferred_element_type=jnp.float32)
    scores = jnp.repeat(scores, per_group, axis=1)
    cum = jnp.cumsum(log_retain.reshape(block_count, SPAN, head_count), axis=1)
    cum_heads = jnp.transpose(cum, (0, 2, 1))
    later_pos = lax.broadcasted_iota(jnp.int32, (SPAN, SPAN), 0)
    earlier_pos = lax.broadcasted_iota(jnp.int32, (SPAN, SPAN), 1)
    causal = later_pos >= earlier_pos
    gap = cum_heads[:, :, :, None] - cum_heads[:, :, None, :]
    mixing = (jnp.where(causal, jnp.exp(jnp.where(causal, gap, 0.0)), 0.0) * scores).astype(
        jnp.bfloat16
    )
    intra = jnp.einsum("khls,kshp->klhp", mixing, inputs, preferred_element_type=jnp.float32)
    tail_decay = jnp.exp(cum_heads[:, :, -1:] - cum_heads)
    b_heads = jnp.repeat(b_grouped, per_group, axis=2)
    weighted_b = (
        b_heads.astype(jnp.float32) * jnp.transpose(tail_decay, (0, 2, 1))[..., None]
    ).astype(jnp.bfloat16)
    block_state = jnp.einsum(
        "klhn,klhp->khnp", weighted_b, inputs, preferred_element_type=jnp.float32
    )
    block_decay = cum_heads[:, :, -1]

    device_state = jnp.zeros((head_count, state_width, head_width), jnp.float32)
    starts_list = []
    for block in range(block_count):
        starts_list.append(device_state)
        device_state = (
            jnp.exp(block_decay[block])[:, None, None] * device_state + block_state[block]
        )
    local_starts = jnp.stack(starts_list)
    device_decay = jnp.sum(block_decay, axis=0)
    total_decay, incoming = shift_scan(
        device_decay, device_state.reshape(head_count, state_width * head_width), "seq"
    )
    incoming = incoming.reshape(head_count, state_width, head_width)
    before_block = jnp.cumsum(block_decay, axis=0) - block_decay
    starts = local_starts + jnp.exp(before_block)[:, :, None, None] * incoming[None]
    c_heads = jnp.repeat(c_grouped, per_group, axis=2).astype(jnp.float32)
    carried = jnp.einsum("klhn,khnp->klhp", c_heads, starts, precision=lax.Precision.HIGHEST)
    carried = carried * jnp.exp(cum)[..., None]
    mixed = intra + carried + skip_d[None, None, :, None] * inputs.astype(jnp.float32)
    gated = mixed * jax.nn.silu(
        gate_z.reshape(block_count, SPAN, head_count, head_width).astype(jnp.float32)
    )
    grouped = gated.reshape(seq_rows, group_count, per_group * head_width)
    grouped = grouped * lax.rsqrt(jnp.mean(grouped * grouped, axis=-1, keepdims=True) + 1e-05)
    ssd_out = (grouped.reshape(seq_rows, channels) * norm_gain[None, :]).astype(jnp.bfloat16)
    w_in_all = lax.all_gather(w_in, "seq", axis=0, tiled=True)
    ssd_out, w_in_all = lax.optimization_barrier((ssd_out, w_in_all))
    own_rows = residual.shape[0]
    mine = lax.axis_index("head")
    residual_rows = lax.dynamic_update_slice_in_dim(
        jnp.zeros((seq_rows, residual.shape[1]), jnp.float32),
        residual.astype(jnp.float32),
        mine * own_rows,
        axis=0,
    )
    partial_sum = jnp.dot(
        ssd_out,
        lax.all_gather(w_out, "seq", axis=1, tiled=True),
        preferred_element_type=jnp.float32,
    )
    with_residual = (partial_sum + residual_rows).astype(jnp.bfloat16)
    hidden = lax.psum(with_residual, "head").astype(jnp.float32)
    unit = refusal / jnp.sqrt(jnp.sum(refusal * refusal) + 1e-06)
    coef = jnp.dot(hidden, unit, precision=lax.Precision.HIGHEST)
    stream_all = (hidden - coef[:, None] * unit[None, :]).astype(jnp.bfloat16)
    stream_float = stream_all.astype(jnp.float32)
    all_rows = (
        stream_float
        * lax.rsqrt(jnp.mean(stream_float * stream_float, axis=-1, keepdims=True) + 1e-05)
        * stream_gain[None, :]
    ).astype(jnp.bfloat16)
    stream = lax.dynamic_slice_in_dim(stream_all, mine * own_rows, own_rows)
    next_float = jnp.dot(
        all_rows,
        w_in_all,
        preferred_element_type=jnp.float32,
    )
    return (stream, next_float.astype(jnp.bfloat16))


def solution(mesh):
    in_specs = (
        P("seq", "head"),
        P("seq", "head"),
        P("seq", "head", None),
        P("seq", "head", None),
        P("seq", "head"),
        P("head"),
        P("head"),
        P("head", "seq"),
        P(("seq", "head"), None),
        P(),
        P(),
        P("seq", "head"),
    )
    out_specs = (P(("seq", "head"), None), P("seq", "head"))
    return jax.shard_map(body, mesh=mesh, in_specs=in_specs, out_specs=out_specs, check_vma=False)
```

```python
import jax
import jax.numpy as jnp
from jax import lax
from jax.sharding import PartitionSpec as P

SPAN = 256


def shift_scan(decay, state, axis):
    devices = lax.axis_size(axis)

    def shifted(parts, distance):
        pairs = [(i, i + distance) for i in range(devices - distance)]
        a, s = parts
        return (
            lax.ppermute(a, axis, pairs),
            lax.ppermute(s.astype(jnp.bfloat16), axis, pairs).astype(jnp.float32),
        )

    acc = shifted((decay, state), 1)
    distance = 1
    while distance < devices:
        acc = carry_combine(shifted(acc, distance), acc)
        distance *= 2
    return acc


def carry_combine(earlier, later):
    decay_early, state_early = earlier
    decay_later, state_later = later
    return (
        decay_early + decay_later,
        jnp.exp(decay_later).reshape((-1,) + (1,) * (state_later.ndim - 1)) * state_early
        + state_later,
    )


def body(
    xin,
    gate_z,
    b_proj,
    c_proj,
    log_retain,
    skip_d,
    norm_gain,
    w_out,
    residual,
    refusal,
    stream_gain,
    w_in,
):
    seq_rows, channels = xin.shape
    head_count = log_retain.shape[1]
    head_width = channels // head_count
    group_count = b_proj.shape[1]
    state_width = b_proj.shape[2]
    per_group = head_count // group_count
    block_count = seq_rows // SPAN
    inputs = xin.reshape(block_count, SPAN, head_count, head_width)
    b_grouped = b_proj.reshape(block_count, SPAN, group_count, state_width)
    c_grouped = c_proj.reshape(block_count, SPAN, group_count, state_width)
    scores = jnp.einsum("klgn,ksgn->kgls", c_grouped, b_grouped, preferred_element_type=jnp.float32)
    scores = jnp.repeat(scores, per_group, axis=1)
    cum = jnp.cumsum(log_retain.reshape(block_count, SPAN, head_count), axis=1)
    cum_heads = jnp.transpose(cum, (0, 2, 1))
    later_pos = lax.broadcasted_iota(jnp.int32, (SPAN, SPAN), 0)
    earlier_pos = lax.broadcasted_iota(jnp.int32, (SPAN, SPAN), 1)
    causal = later_pos >= earlier_pos
    gap = cum_heads[:, :, :, None] - cum_heads[:, :, None, :]
    mixing = (jnp.where(causal, jnp.exp(jnp.where(causal, gap, 0.0)), 0.0) * scores).astype(
        jnp.bfloat16
    )
    intra = jnp.einsum("khls,kshp->klhp", mixing, inputs, preferred_element_type=jnp.float32)
    tail_decay = jnp.exp(cum_heads[:, :, -1:] - cum_heads)
    b_heads = jnp.repeat(b_grouped, per_group, axis=2)
    weighted_b = (
        b_heads.astype(jnp.float32) * jnp.transpose(tail_decay, (0, 2, 1))[..., None]
    ).astype(jnp.bfloat16)
    block_state = jnp.einsum(
        "klhn,klhp->khnp", weighted_b, inputs, preferred_element_type=jnp.float32
    )
    block_decay = cum_heads[:, :, -1]

    device_state = jnp.zeros((head_count, state_width, head_width), jnp.float32)
    starts_list = []
    for block in range(block_count):
        starts_list.append(device_state)
        device_state = (
            jnp.exp(block_decay[block])[:, None, None] * device_state + block_state[block]
        )
    local_starts = jnp.stack(starts_list)
    device_decay = jnp.sum(block_decay, axis=0)
    total_decay, incoming = shift_scan(
        device_decay, device_state.reshape(head_count, state_width * head_width), "seq"
    )
    incoming = incoming.reshape(head_count, state_width, head_width)
    before_block = jnp.cumsum(block_decay, axis=0) - block_decay
    starts = local_starts + jnp.exp(before_block)[:, :, None, None] * incoming[None]
    c_heads = jnp.repeat(c_grouped, per_group, axis=2).astype(jnp.float32)
    carried = jnp.einsum("klhn,khnp->klhp", c_heads, starts, precision=lax.Precision.HIGHEST)
    carried = carried * jnp.exp(cum)[..., None]
    mixed = intra + carried + skip_d[None, None, :, None] * inputs.astype(jnp.float32)
    gated = mixed * jax.nn.silu(
        gate_z.reshape(block_count, SPAN, head_count, head_width).astype(jnp.float32)
    )
    grouped = gated.reshape(seq_rows, group_count, per_group * head_width)
    grouped = grouped * lax.rsqrt(jnp.mean(grouped * grouped, axis=-1, keepdims=True) + 1e-05)
    ssd_out = (grouped.reshape(seq_rows, channels) * norm_gain[None, :]).astype(jnp.bfloat16)
    w_in_all = lax.all_gather(w_in, "seq", axis=0, tiled=True)
    ssd_out, w_in_all = lax.optimization_barrier((ssd_out, w_in_all))
    own_rows = residual.shape[0]
    mine = lax.axis_index("head")
    residual_rows = lax.dynamic_update_slice_in_dim(
        jnp.zeros((seq_rows, residual.shape[1]), jnp.float32),
        residual.astype(jnp.float32),
        mine * own_rows,
        axis=0,
    )
    partial_sum = jnp.dot(
        ssd_out,
        lax.all_gather(w_out, "seq", axis=1, tiled=True),
        preferred_element_type=jnp.float32,
    )
    with_residual = (partial_sum + residual_rows).astype(jnp.bfloat16)
    hidden = lax.psum(with_residual, "head").astype(jnp.float32)
    unit = refusal / jnp.sqrt(jnp.sum(refusal * refusal) + 1e-06)
    coef = jnp.dot(hidden, unit, precision=lax.Precision.HIGH)
    stream_all = (hidden - coef[:, None] * unit[None, :]).astype(jnp.bfloat16)
    stream_float = stream_all.astype(jnp.float32)
    all_rows = (
        stream_float
        * lax.rsqrt(jnp.mean(stream_float * stream_float, axis=-1, keepdims=True) + 1e-05)
        * stream_gain[None, :]
    ).astype(jnp.bfloat16)
    stream = lax.dynamic_slice_in_dim(stream_all, mine * own_rows, own_rows)
    next_float = jnp.dot(
        all_rows,
        w_in_all,
        preferred_element_type=jnp.float32,
    )
    return (stream, next_float.astype(jnp.bfloat16))


def solution(mesh):
    in_specs = (
        P("seq", "head"),
        P("seq", "head"),
        P("seq", "head", None),
        P("seq", "head", None),
        P("seq", "head"),
        P("head"),
        P("head"),
        P("head", "seq"),
        P(("seq", "head"), None),
        P(),
        P(),
        P("seq", "head"),
    )
    out_specs = (P(("seq", "head"), None), P("seq", "head"))
    return jax.shard_map(body, mesh=mesh, in_specs=in_specs, out_specs=out_specs, check_vma=False)
```

```python
import jax
import jax.numpy as jnp
from jax import lax
from jax.sharding import PartitionSpec as P

SPAN = 256


def shift_scan(decay, state, axis):
    devices = lax.axis_size(axis)

    def shifted(parts, distance):
        pairs = [(i, i + distance) for i in range(devices - distance)]
        a, s = parts
        return (
            lax.ppermute(a, axis, pairs),
            lax.ppermute(s.astype(jnp.bfloat16), axis, pairs).astype(jnp.float32),
        )

    acc = shifted((decay, state), 1)
    distance = 1
    while distance < devices:
        acc = carry_combine(shifted(acc, distance), acc)
        distance *= 2
    return acc


def carry_combine(earlier, later):
    decay_early, state_early = earlier
    decay_later, state_later = later
    return (
        decay_early + decay_later,
        jnp.exp(decay_later).reshape((-1,) + (1,) * (state_later.ndim - 1)) * state_early
        + state_later,
    )


def body(
    xin,
    gate_z,
    b_proj,
    c_proj,
    log_retain,
    skip_d,
    norm_gain,
    w_out,
    residual,
    refusal,
    stream_gain,
    w_in,
):
    seq_rows, channels = xin.shape
    head_count = log_retain.shape[1]
    head_width = channels // head_count
    group_count = b_proj.shape[1]
    state_width = b_proj.shape[2]
    per_group = head_count // group_count
    block_count = seq_rows // SPAN
    inputs = xin.reshape(block_count, SPAN, head_count, head_width)
    b_grouped = b_proj.reshape(block_count, SPAN, group_count, state_width)
    c_grouped = c_proj.reshape(block_count, SPAN, group_count, state_width)
    scores = jnp.einsum("klgn,ksgn->kgls", c_grouped, b_grouped, preferred_element_type=jnp.float32)
    scores = jnp.repeat(scores, per_group, axis=1)
    cum = jnp.cumsum(log_retain.reshape(block_count, SPAN, head_count), axis=1)
    cum_heads = jnp.transpose(cum, (0, 2, 1))
    later_pos = lax.broadcasted_iota(jnp.int32, (SPAN, SPAN), 0)
    earlier_pos = lax.broadcasted_iota(jnp.int32, (SPAN, SPAN), 1)
    causal = later_pos >= earlier_pos
    gap = cum_heads[:, :, :, None] - cum_heads[:, :, None, :]
    mixing = (jnp.where(causal, jnp.exp(jnp.where(causal, gap, 0.0)), 0.0) * scores).astype(
        jnp.bfloat16
    )
    intra = jnp.einsum("khls,kshp->klhp", mixing, inputs, preferred_element_type=jnp.float32)
    tail_decay = jnp.exp(cum_heads[:, :, -1:] - cum_heads)
    b_heads = jnp.repeat(b_grouped, per_group, axis=2)
    weighted_b = (
        b_heads.astype(jnp.float32) * jnp.transpose(tail_decay, (0, 2, 1))[..., None]
    ).astype(jnp.bfloat16)
    block_state = jnp.einsum(
        "klhn,klhp->khnp", weighted_b, inputs, preferred_element_type=jnp.float32
    )
    block_decay = cum_heads[:, :, -1]

    device_state = jnp.zeros((head_count, state_width, head_width), jnp.float32)
    starts_list = []
    for block in range(block_count):
        starts_list.append(device_state)
        device_state = (
            jnp.exp(block_decay[block])[:, None, None] * device_state + block_state[block]
        )
    local_starts = jnp.stack(starts_list)
    device_decay = jnp.sum(block_decay, axis=0)
    total_decay, incoming = shift_scan(
        device_decay, device_state.reshape(head_count, state_width * head_width), "seq"
    )
    incoming = incoming.reshape(head_count, state_width, head_width)
    before_block = jnp.cumsum(block_decay, axis=0) - block_decay
    starts = local_starts + jnp.exp(before_block)[:, :, None, None] * incoming[None]
    c_heads = jnp.repeat(c_grouped, per_group, axis=2).astype(jnp.float32)
    carried = jnp.einsum("klhn,khnp->klhp", c_heads, starts, precision=lax.Precision.HIGHEST)
    carried = carried * jnp.exp(cum)[..., None]
    mixed = intra + carried + skip_d[None, None, :, None] * inputs.astype(jnp.float32)
    gated = mixed * jax.nn.silu(
        gate_z.reshape(block_count, SPAN, head_count, head_width).astype(jnp.float32)
    )
    grouped = gated.reshape(seq_rows, group_count, per_group * head_width)
    grouped = grouped * lax.rsqrt(jnp.mean(grouped * grouped, axis=-1, keepdims=True) + 1e-05)
    ssd_out = (grouped.reshape(seq_rows, channels) * norm_gain[None, :]).astype(jnp.bfloat16)
    w_in_all = lax.all_gather(w_in, "seq", axis=0, tiled=True)
    ssd_out, w_in_all = lax.optimization_barrier((ssd_out, w_in_all))
    own_rows = residual.shape[0]
    mine = lax.axis_index("head")
    head_devices = seq_rows // own_rows
    in_block = lax.broadcasted_iota(jnp.int32, (head_devices, 1, 1), 0) == mine
    residual_rows = jnp.where(
        in_block, residual.astype(jnp.float32)[None], 0.0
    ).reshape(seq_rows, residual.shape[1])
    partial_sum = jnp.dot(
        ssd_out,
        lax.all_gather(w_out, "seq", axis=1, tiled=True),
        preferred_element_type=jnp.float32,
    )
    with_residual = (partial_sum + residual_rows).astype(jnp.bfloat16)
    hidden = lax.psum(with_residual, "head").astype(jnp.float32)
    unit = refusal / jnp.sqrt(jnp.sum(refusal * refusal) + 1e-06)
    coef = jnp.dot(hidden, unit, precision=lax.Precision.HIGH)
    stream_all = (hidden - coef[:, None] * unit[None, :]).astype(jnp.bfloat16)
    stream_float = stream_all.astype(jnp.float32)
    all_rows = (
        stream_float
        * lax.rsqrt(jnp.mean(stream_float * stream_float, axis=-1, keepdims=True) + 1e-05)
        * stream_gain[None, :]
    ).astype(jnp.bfloat16)
    stream = lax.dynamic_slice_in_dim(stream_all, mine * own_rows, own_rows)
    next_float = jnp.dot(
        all_rows,
        w_in_all,
        preferred_element_type=jnp.float32,
    )
    return (stream, next_float.astype(jnp.bfloat16))


def solution(mesh):
    in_specs = (
        P("seq", "head"),
        P("seq", "head"),
        P("seq", "head", None),
        P("seq", "head", None),
        P("seq", "head"),
        P("head"),
        P("head"),
        P("head", "seq"),
        P(("seq", "head"), None),
        P(),
        P(),
        P("seq", "head"),
    )
    out_specs = (P(("seq", "head"), None), P("seq", "head"))
    return jax.shard_map(body, mesh=mesh, in_specs=in_specs, out_specs=out_specs, check_vma=False)
```
